256 devices in a mesh: seq: 8 (over x, core), chan: 32 (over y, z).
Axes of the slice: x: 4, y: 4, z: 8, core: 2. Of those that a mesh axis runs over, the one named last changes fastest.
Arguments:
- query_input: bfloat16 [512, 65536], P('chan', 'seq'), may hold values from -6 to 6
- key_input: bfloat16 [512, 65536], P('chan', 'seq'), may hold values from -6 to 6
- value_input: bfloat16 [512, 65536], P('chan', 'seq'), may hold values from -6 to 6
- short_taps: float32 [3, 3, 512], P(None, None, 'chan'), may hold values from -3 to 3
- long_filter: float32 [512, 65536], P('chan', 'seq'), may hold values from -0.0234375 to 0.0234375
- skip_gain: float32 [512], P('chan'), may hold values from -4 to 4
- output_weight: bfloat16 [8192, 512], P('chan'), may hold values from -0.25 to 0.25
Outputs:
- mixed_out: bfloat16 [8192, 65536], P('chan', 'seq')
The draws below stay inside these ranges and needn't reach their ends.
All inputs are finite; a program needn't handle non-finite values.
Results may differ from the reference program's by a relative error of at most 0.0049.
Values may be sent and summed in bfloat16 or wider, within the bound.
No kernel may reach another device: no remote copies, remote signals or barrier semaphores. Data moves between devices by JAX's collectives and lax.ppermute only.
A program may use at most 128 MiB of HBM per device.

```python
import jax
import jax.numpy as jnp
from jax import lax

MODEL_WIDTH = 8192
CHANNELS = 512
SEQ = 65536


def block_levels(own_key, extent, split, least, top_value):
    level, own = 1.0, jax.random.fold_in(own_key, 6)
    for position, blocks in split:
        heights = jnp.exp(jax.random.uniform(jax.random.fold_in(own, position), (blocks,), jnp.float32, least / len(split), top_value / len(split)))
        level = level * jnp.repeat(heights, extent[position] // blocks).reshape([-1 if axis == position else 1 for axis in range(len(extent))])
    return level


def scatter_about(key, dims, width, most, cuts=(), kind=jnp.bfloat16):
    array = jax.random.normal(key, dims, jnp.float32) * width
    if len(cuts) > 0:
        array = block_levels(key, dims, cuts, -0.22, 0.18) * array
    return jnp.clip(array, min=-most, max=most).astype(kind)


def setup_inputs(seed: int = 0) -> dict:
    key_of = jax.random.split(jax.random.key(seed), 8)
    query_input = scatter_about(key_of[0], (CHANNELS, SEQ), 1.0, 6.0, ((0, 32), (1, 8)))
    key_input = scatter_about(key_of[1], (CHANNELS, SEQ), 1.0, 6.0, ((0, 32), (1, 8)))
    value_input = scatter_about(key_of[2], (CHANNELS, SEQ), 1.0, 6.0, ((0, 32), (1, 8)))
    short_taps = scatter_about(key_of[3], (3, 3, CHANNELS), 0.6, 3.0, ((2, 32),), jnp.float32)
    long_filter = scatter_about(key_of[4], (CHANNELS, SEQ), (SEQ ** -0.5), 0.0234375, ((0, 32), (1, 8)), jnp.float32)
    skip_gain = scatter_about(key_of[5], (CHANNELS,), 1.0, 4.0, ((0, 32),), jnp.float32)
    output_weight = scatter_about(key_of[6], (MODEL_WIDTH, CHANNELS), CHANNELS ** -0.5, 0.25, ((0, 32),))
    return dict(query_input=query_input, key_input=key_input, value_input=value_input, short_taps=short_taps, long_filter=long_filter, skip_gain=skip_gain, output_weight=output_weight)


def spectral(filter_pairs):
    padded_length = 2 * SEQ
    spectra = jnp.fft.rfft(filter_pairs, n=padded_length, axis=-1)
    return jnp.fft.irfft(spectra[0] * spectra[1], n=padded_length, axis=-1)[:, :SEQ]


def reference(query_input, key_input, value_input, short_taps, long_filter, skip_gain, output_weight):
    stacked = jnp.stack([query_input, key_input, value_input]).astype(jnp.float32)
    padded = jnp.pad(stacked, ((0, 0), (0, 0), (2, 0)))
    featured = short_taps[0][:, :, None] * padded[:, :, 2:] + short_taps[1][:, :, None] * padded[:, :, 1:-1] + short_taps[2][:, :, None] * padded[:, :, :-2]
    query_part = featured[0]
    key_value = featured[1] * featured[2]
    filter_pairs = jnp.stack([key_value, long_filter]).reshape(2, CHANNELS // 8, 8, SEQ).transpose(1, 0, 2, 3)
    convolved = lax.map(spectral, filter_pairs).reshape(CHANNELS, SEQ)
    gated = (query_part * (convolved + skip_gain[:, None] * key_value)).astype(jnp.bfloat16)
    return jnp.dot(output_weight, gated, preferred_element_type=jnp.float32).astype(jnp.bfloat16)
```

```python
import numpy as np

import jax
import jax.numpy as jnp
from jax import lax
from jax.sharding import PartitionSpec as P

exactness = lax.Precision.HIGH
BLOCK = 256


def from_behind(value, axis, by):
    count = lax.axis_size(axis)
    pairs = [(i, i + by) for i in range(count) if 0 <= i + by < count]
    return lax.ppermute(value, axis, pairs)


def dft_tables(seq_length):
    rows = 2 * seq_length // BLOCK
    half = seq_length // BLOCK
    k1 = np.arange(rows)[:, None]
    n1 = np.arange(half)[None, :]
    col = np.arange(BLOCK)
    first = 2.0 * np.pi * ((k1 * n1) % rows) / rows
    second = 2.0 * np.pi * ((col[:, None] * col[None, :]) % BLOCK) / BLOCK
    turn = 2.0 * np.pi * (k1 * col[None, :]) / (2 * seq_length)
    pair = lambda a: (jnp.asarray(np.cos(a), jnp.float32), jnp.asarray(np.sin(a), jnp.float32))
    return pair(first), pair(second), pair(turn)


def mm(a, b):
    return jnp.matmul(a, b, precision=exactness)


def spectral_conv(series, filters):
    channels, seq_length = series.shape
    (c1, s1), (c2, s2), (ct, st) = dft_tables(seq_length)
    half = seq_length // BLOCK
    signals = 2 * channels
    stacked = jnp.stack([series, filters]).reshape(signals, half, BLOCK)
    stacked = jnp.transpose(stacked, (1, 0, 2)).reshape(half, signals * BLOCK)
    a_re = mm(c1, stacked).reshape(-1, signals, BLOCK)
    a_im = -mm(s1, stacked).reshape(-1, signals, BLOCK)
    t_re = (a_re * ct[:, None, :] + a_im * st[:, None, :]).reshape(-1, BLOCK)
    t_im = (a_im * ct[:, None, :] - a_re * st[:, None, :]).reshape(-1, BLOCK)
    b_re = (mm(t_re, c2) + mm(t_im, s2)).reshape(-1, 2, channels, BLOCK)
    b_im = (mm(t_im, c2) - mm(t_re, s2)).reshape(-1, 2, channels, BLOCK)
    p_re = (b_re[:, 0] * b_re[:, 1] - b_im[:, 0] * b_im[:, 1]).reshape(-1, BLOCK)
    p_im = (b_re[:, 0] * b_im[:, 1] + b_im[:, 0] * b_re[:, 1]).reshape(-1, BLOCK)
    q_re = (mm(p_re, c2) - mm(p_im, s2)).reshape(-1, channels, BLOCK)
    q_im = (mm(p_im, c2) + mm(p_re, s2)).reshape(-1, channels, BLOCK)
    u_re = (q_re * ct[:, None, :] - q_im * st[:, None, :]).reshape(-1, channels * BLOCK)
    u_im = (q_im * ct[:, None, :] + q_re * st[:, None, :]).reshape(-1, channels * BLOCK)
    back = mm(c1.T, u_re) - mm(s1.T, u_im)
    back = jnp.transpose(back.reshape(half, channels, BLOCK), (1, 0, 2)).reshape(channels, seq_length)
    return back * (1.0 / (2 * seq_length))


def whole_conv(key_value, long_filter):
    joined = jnp.stack([key_value, long_filter])
    regrouped = lax.all_to_all(joined, "seq", split_axis=1, concat_axis=2, tiled=True)
    series = spectral_conv(regrouped[0], regrouped[1])
    return lax.all_to_all(series, "seq", split_axis=1, concat_axis=0, tiled=True)


def shards(query_input, key_input, value_input, short_taps, long_filter, skip_gain, output_weight):
    channels, positions = query_input.shape
    stacked = jnp.stack([query_input, key_input, value_input])
    before = from_behind(stacked[:, :, positions - 2 :], "seq", 1)
    extended = jnp.concatenate([before, stacked], axis=2).astype(jnp.float32)
    featured = (
        short_taps[0][:, :, None] * extended[:, :, 2:]
        + short_taps[1][:, :, None] * extended[:, :, 1:-1]
        + short_taps[2][:, :, None] * extended[:, :, :-2]
    )
    query_part = featured[0]
    key_value = featured[1] * featured[2]
    convolved = whole_conv(key_value, long_filter)
    gated = (query_part * (convolved + skip_gain[:, None] * key_value)).astype(jnp.bfloat16)
    result = jnp.dot(
        output_weight,
        lax.all_gather(gated, "chan", axis=0, tiled=True),
        preferred_element_type=jnp.float32,
    )
    return result.astype(jnp.bfloat16)


def solution(mesh):
    return jax.shard_map(
        shards,
        mesh=mesh,
        in_specs=(
            P("chan", "seq"),
            P("chan", "seq"),
            P("chan", "seq"),
            P(None, None, "chan"),
            P("chan", "seq"),
            P("chan"),
            P("chan", None),
        ),
        out_specs=P("chan", "seq"),
        check_vma=False,
    )
```

```python
import numpy as np

import jax
import jax.numpy as jnp
from jax import lax
from jax.sharding import Mesh, PartitionSpec as P

exactness = lax.Precision.HIGH
BLOCK = 256


def from_behind(value, axis, by):
    count = lax.axis_size(axis)
    pairs = [(i, i + by) for i in range(count) if 0 <= i + by < count]
    return lax.ppermute(value, axis, pairs)


def dft_tables(seq_length):
    rows = 2 * seq_length // BLOCK
    half = seq_length // BLOCK
    k1 = np.arange(rows)[:, None]
    n1 = np.arange(half)[None, :]
    col = np.arange(BLOCK)
    first = 2.0 * np.pi * ((k1 * n1) % rows) / rows
    second = 2.0 * np.pi * ((col[:, None] * col[None, :]) % BLOCK) / BLOCK
    turn = 2.0 * np.pi * (k1 * col[None, :]) / (2 * seq_length)
    pair = lambda a: (jnp.asarray(np.cos(a), jnp.float32), jnp.asarray(np.sin(a), jnp.float32))
    return pair(first), pair(second), pair(turn)


def mm(a, b):
    return jnp.matmul(a, b, precision=exactness)


def spectral_conv(series, filters):
    channels, seq_length = series.shape
    (c1, s1), (c2, s2), (ct, st) = dft_tables(seq_length)
    half = seq_length // BLOCK
    signals = 2 * channels
    stacked = jnp.stack([series, filters]).reshape(signals, half, BLOCK)
    stacked = jnp.transpose(stacked, (1, 0, 2)).reshape(half, signals * BLOCK)
    a_re = mm(c1, stacked).reshape(-1, signals, BLOCK)
    a_im = -mm(s1, stacked).reshape(-1, signals, BLOCK)
    t_re = (a_re * ct[:, None, :] + a_im * st[:, None, :]).reshape(-1, BLOCK)
    t_im = (a_im * ct[:, None, :] - a_re * st[:, None, :]).reshape(-1, BLOCK)
    b_re = (mm(t_re, c2) + mm(t_im, s2)).reshape(-1, 2, channels, BLOCK)
    b_im = (mm(t_im, c2) - mm(t_re, s2)).reshape(-1, 2, channels, BLOCK)
    p_re = (b_re[:, 0] * b_re[:, 1] - b_im[:, 0] * b_im[:, 1]).reshape(-1, BLOCK)
    p_im = (b_re[:, 0] * b_im[:, 1] + b_im[:, 0] * b_re[:, 1]).reshape(-1, BLOCK)
    q_re = (mm(p_re, c2) - mm(p_im, s2)).reshape(-1, channels, BLOCK)
    q_im = (mm(p_im, c2) + mm(p_re, s2)).reshape(-1, channels, BLOCK)
    u_re = (q_re * ct[:, None, :] - q_im * st[:, None, :]).reshape(-1, channels * BLOCK)
    u_im = (q_im * ct[:, None, :] + q_re * st[:, None, :]).reshape(-1, channels * BLOCK)
    back = mm(c1.T, u_re) - mm(s1.T, u_im)
    back = jnp.transpose(back.reshape(half, channels, BLOCK), (1, 0, 2)).reshape(channels, seq_length)
    return back * (1.0 / (2 * seq_length))


def whole_conv(key_value, long_filter):
    joined = jnp.stack([key_value, long_filter])
    regrouped = lax.all_to_all(joined, ("sx", "sc"), split_axis=1, concat_axis=2, tiled=True)
    series = spectral_conv(regrouped[0], regrouped[1])
    return lax.all_to_all(series, ("sx", "sc"), split_axis=1, concat_axis=0, tiled=True)


def shift(value, axis, by):
    count = lax.axis_size(axis)
    return lax.ppermute(value, axis, [(i, (i + by) % count) for i in range(count)])


def ring_gather(piece, axis, split_axis):
    count = lax.axis_size(axis)
    ahead, behind = [piece], [piece]
    for _ in range((count - 1) // 2):
        ahead.append(shift(ahead[-1], axis, -1))
        behind.append(shift(behind[-1], axis, 1))
    order = ahead
    if count % 2 == 0:
        cut = piece.shape[split_axis] // 2
        low = shift(lax.slice_in_dim(behind[-1], 0, cut, axis=split_axis), axis, 1)
        high = shift(lax.slice_in_dim(ahead[-1], cut, None, axis=split_axis), axis, -1)
        order = order + [jnp.concatenate([low, high], axis=split_axis)]
    order = order + behind[1:][::-1]
    return jnp.stack(order)


def rolled_weight(output_weight, first, second):
    rows = output_weight.shape[0]
    size_y, size_z = lax.axis_size("cy"), lax.axis_size("cz")
    grid = output_weight.reshape(rows, size_y, size_z, -1)
    grid = jnp.roll(grid, -lax.axis_index("cy"), axis=1)
    grid = jnp.roll(grid, -lax.axis_index("cz"), axis=2)
    if first == "cy":
        grid = jnp.swapaxes(grid, 1, 2)
    return grid.reshape(rows, -1)


def project(gated, output_weight):
    positions = gated.shape[1]
    cut = positions * 9 // 16
    results = []
    for first, second, part in (("cz", "cy", gated[:, :cut]), ("cy", "cz", gated[:, cut:])):
        inner = ring_gather(part, first, 1)
        outer = ring_gather(inner, second, 2)
        stacked = outer.reshape(-1, part.shape[1])
        weight = rolled_weight(output_weight, first, second)
        results.append(jnp.dot(weight, stacked, preferred_element_type=jnp.float32))
    return jnp.concatenate(results, axis=1).astype(jnp.bfloat16)


def shards(query_input, key_input, value_input, short_taps, long_filter, skip_gain, output_weight):
    channels, positions = query_input.shape
    stacked = jnp.stack([query_input, key_input, value_input])
    before = from_behind(stacked[:, :, positions - 2 :], ("sx", "sc"), 1)
    extended = jnp.concatenate([before, stacked], axis=2).astype(jnp.float32)
    featured = (
        short_taps[0][:, :, None] * extended[:, :, 2:]
        + short_taps[1][:, :, None] * extended[:, :, 1:-1]
        + short_taps[2][:, :, None] * extended[:, :, :-2]
    )
    query_part = featured[0]
    key_value = featured[1] * featured[2]
    convolved = whole_conv(key_value, long_filter)
    gated = (query_part * (convolved + skip_gain[:, None] * key_value)).astype(jnp.bfloat16)
    return project(gated, output_weight)


def solution(mesh):
    seq_size, chan_size = mesh.devices.shape
    z_size = 8 if chan_size % 8 == 0 else chan_size
    grid = Mesh(
        mesh.devices.reshape(seq_size // 2, 2, chan_size // z_size, z_size),
        ("sx", "sc", "cy", "cz"),
    )
    seq = ("sx", "sc")
    chan = ("cy", "cz")
    return jax.shard_map(
        shards,
        mesh=grid,
        in_specs=(
            P(chan, seq),
            P(chan, seq),
            P(chan, seq),
            P(None, None, chan),
            P(chan, seq),
            P(chan),
            P(chan, None),
        ),
        out_specs=P(chan, seq),
        check_vma=False,
    )
```

```python
import numpy as np

import jax
import jax.numpy as jnp
from jax import lax
from jax.sharding import Mesh, PartitionSpec as P

exactness = lax.Precision.HIGH
BLOCK = 256


def from_behind(value, axis, by):
    count = lax.axis_size(axis)
    pairs = [(i, i + by) for i in range(count) if 0 <= i + by < count]
    return lax.ppermute(value, axis, pairs)


def dft_tables(seq_length):
    rows = 2 * seq_length // BLOCK
    half = seq_length // BLOCK
    k1 = np.arange(rows)[:, None]
    n1 = np.arange(half)[None, :]
    col = np.arange(BLOCK)
    first = 2.0 * np.pi * ((k1 * n1) % rows) / rows
    second = 2.0 * np.pi * ((col[:, None] * col[None, :]) % BLOCK) / BLOCK
    turn = 2.0 * np.pi * (k1 * col[None, :]) / (2 * seq_length)
    pair = lambda a: (jnp.asarray(np.cos(a), jnp.float32), jnp.asarray(np.sin(a), jnp.float32))
    return pair(first), pair(second), pair(turn)


def mm(a, b):
    return jnp.matmul(a, b, precision=exactness)


def spectral_conv(series, filters):
    channels, seq_length = series.shape
    (c1, s1), (c2, s2), (ct, st) = dft_tables(seq_length)
    half = seq_length // BLOCK
    signals = 2 * channels
    stacked = jnp.stack([series, filters]).reshape(signals, half, BLOCK)
    stacked = jnp.transpose(stacked, (1, 0, 2)).reshape(half, signals * BLOCK)
    a_re = mm(c1, stacked).reshape(-1, signals, BLOCK)
    a_im = -mm(s1, stacked).reshape(-1, signals, BLOCK)
    t_re = (a_re * ct[:, None, :] + a_im * st[:, None, :]).reshape(-1, BLOCK)
    t_im = (a_im * ct[:, None, :] - a_re * st[:, None, :]).reshape(-1, BLOCK)
    b_re = (mm(t_re, c2) + mm(t_im, s2)).reshape(-1, 2, channels, BLOCK)
    b_im = (mm(t_im, c2) - mm(t_re, s2)).reshape(-1, 2, channels, BLOCK)
    p_re = (b_re[:, 0] * b_re[:, 1] - b_im[:, 0] * b_im[:, 1]).reshape(-1, BLOCK)
    p_im = (b_re[:, 0] * b_im[:, 1] + b_im[:, 0] * b_re[:, 1]).reshape(-1, BLOCK)
    q_re = (mm(p_re, c2) - mm(p_im, s2)).reshape(-1, channels, BLOCK)
    q_im = (mm(p_im, c2) + mm(p_re, s2)).reshape(-1, channels, BLOCK)
    u_re = (q_re * ct[:, None, :] - q_im * st[:, None, :]).reshape(-1, channels * BLOCK)
    u_im = (q_im * ct[:, None, :] + q_re * st[:, None, :]).reshape(-1, channels * BLOCK)
    back = mm(c1.T, u_re) - mm(s1.T, u_im)
    back = jnp.transpose(back.reshape(half, channels, BLOCK), (1, 0, 2)).reshape(channels, seq_length)
    return back * (1.0 / (2 * seq_length))


def whole_conv(key_value, long_filter):
    joined = jnp.stack([key_value, long_filter])
    regrouped = lax.all_to_all(joined, ("sx", "sc"), split_axis=1, concat_axis=2, tiled=True)
    series = spectral_conv(regrouped[0], regrouped[1])
    return lax.all_to_all(series, ("sx", "sc"), split_axis=1, concat_axis=0, tiled=True)


def shift(value, axis, by):
    count = lax.axis_size(axis)
    return lax.ppermute(value, axis, [(i, (i + by) % count) for i in range(count)])


def ring_gather(piece, axis, split_axis):
    count = lax.axis_size(axis)
    ahead, behind = [piece], [piece]
    for _ in range((count - 1) // 2):
        ahead.append(shift(ahead[-1], axis, -1))
        behind.append(shift(behind[-1], axis, 1))
    order = ahead
    if count % 2 == 0:
        cut = piece.shape[split_axis] // 2
        low = shift(lax.slice_in_dim(behind[-1], 0, cut, axis=split_axis), axis, 1)
        high = shift(lax.slice_in_dim(ahead[-1], cut, None, axis=split_axis), axis, -1)
        order = order + [jnp.concatenate([low, high], axis=split_axis)]
    order = order + behind[1:][::-1]
    return jnp.stack(order)


def rolled_weight(output_weight, first, second):
    rows = output_weight.shape[0]
    size_y, size_z = lax.axis_size("cy"), lax.axis_size("cz")
    grid = output_weight.reshape(rows, size_y, size_z, -1)
    grid = jnp.roll(grid, -lax.axis_index("cy"), axis=1)
    grid = jnp.roll(grid, -lax.axis_index("cz"), axis=2)
    if first == "cy":
        grid = jnp.swapaxes(grid, 1, 2)
    return grid.reshape(rows, -1)


def project(gated, output_weight):
    positions = gated.shape[1]
    cut = positions * 9 // 16
    results = []
    for first, second, part in (("cz", "cy", gated[:, :cut]), ("cy", "cz", gated[:, cut:])):
        inner = ring_gather(part, first, 1)
        outer = ring_gather(inner, second, 2)
        stacked = outer.reshape(-1, part.shape[1])
        weight = rolled_weight(output_weight, first, second)
        results.append(jnp.dot(weight, stacked, preferred_element_type=jnp.float32))
    return jnp.concatenate(results, axis=1)


def shards(query_input, key_input, value_input, short_taps, long_filter, skip_gain, output_weight):
    channels, positions = query_input.shape
    stacked = jnp.stack([query_input, key_input, value_input])
    before = from_behind(stacked[:, :, positions - 2 :], ("sx", "sc"), 1)
    extended = jnp.concatenate([before, stacked], axis=2).astype(jnp.float32)
    featured = (
        short_taps[0][:, :, None] * extended[:, :, 2:]
        + short_taps[1][:, :, None] * extended[:, :, 1:-1]
        + short_taps[2][:, :, None] * extended[:, :, :-2]
    )
    query_part = featured[0]
    key_value = featured[1] * featured[2]
    rows = output_weight.shape[0]
    groups = 2
    per = channels // groups
    total = None
    previous = None
    for group in range(groups):
        part = slice(group * per, (group + 1) * per)
        series, filters = key_value[part], long_filter[part]
        if previous is not None:
            previous, series, filters = lax.optimization_barrier((previous, series, filters))
        convolved = whole_conv(series, filters)
        gated = (query_part[part] * (convolved + skip_gain[part, None] * key_value[part])).astype(jnp.bfloat16)
        weight = output_weight.reshape(rows, -1, channels)[:, :, part].reshape(rows, -1)
        if group == 0:
            previous = gated
            term = project(gated, weight)
        else:
            gathered = lax.all_gather(gated, ("cy", "cz"), axis=0, tiled=True)
            term = jnp.dot(weight, gathered, preferred_element_type=jnp.float32)
        total = term if total is None else total + term
    return total.astype(jnp.bfloat16)


def solution(mesh):
    seq_size, chan_size = mesh.devices.shape
    z_size = 8 if chan_size % 8 == 0 else chan_size
    grid = Mesh(
        mesh.devices.reshape(seq_size // 2, 2, chan_size // z_size, z_size),
        ("sx", "sc", "cy", "cz"),
    )
    seq = ("sx", "sc")
    chan = ("cy", "cz")
    return jax.shard_map(
        shards,
        mesh=grid,
        in_specs=(
            P(chan, seq),
            P(chan, seq),
            P(chan, seq),
            P(None, None, chan),
            P(chan, seq),
            P(chan),
            P(chan, None),
        ),
        out_specs=P(chan, seq),
        check_vma=False,
    )
```

```python
import numpy as np

import jax
import jax.numpy as jnp
from jax.experimental import pallas as pl
from jax.experimental.pallas import tpu as pltpu
from jax import lax
from jax.sharding import Mesh, PartitionSpec as P

INTERPRET = False
BLOCK = 256


def from_behind(value, axis, by):
    count = lax.axis_size(axis)
    pairs = [(i, i + by) for i in range(count) if 0 <= i + by < count]
    return lax.ppermute(value, axis, pairs)


def dft_tables(seq_length):
    rows = 2 * seq_length // BLOCK
    half = seq_length // BLOCK
    k1 = np.arange(rows)[:, None]
    n1 = np.arange(half)[None, :]
    col = np.arange(BLOCK)
    first = 2.0 * np.pi * ((k1 * n1) % rows) / rows
    second = 2.0 * np.pi * ((col[:, None] * col[None, :]) % BLOCK) / BLOCK
    turn = 2.0 * np.pi * (k1 * col[None, :]) / (2 * seq_length)

    def halves(table):
        table = np.asarray(table, np.float32)
        high = table.astype(jnp.bfloat16)
        low = (table - high.astype(np.float32)).astype(jnp.bfloat16)
        return [jnp.asarray(high), jnp.asarray(low)]

    tables = []
    for table in (np.cos(first), np.sin(first), np.cos(second), np.sin(second), np.cos(first).T, np.sin(first).T):
        tables += halves(table)
    tables += [jnp.asarray(np.cos(turn), jnp.float32), jnp.asarray(np.sin(turn), jnp.float32)]
    return tables


def split3(value):
    high = value.astype(jnp.bfloat16)
    return high, (value - high.astype(jnp.float32)).astype(jnp.bfloat16)


def dot3(a, b):
    def one(p, q):
        return jnp.dot(p, q, preferred_element_type=jnp.float32)

    return one(a[0], b[0]) + (one(a[0], b[1]) + one(a[1], b[0]))


def conv_kernel(x_ref, c1h, c1l, s1h, s1l, c2h, c2l, s2h, s2l, c1th, c1tl, s1th, s1tl, ct_ref, st_ref, o_ref):
    channels = o_ref.shape[0]
    scale = 1.0 / (2 * x_ref.shape[1] * x_ref.shape[2])
    c1, s1 = (c1h[...], c1l[...]), (s1h[...], s1l[...])
    c2, s2 = (c2h[...], c2l[...]), (s2h[...], s2l[...])
    ct, st = ct_ref[...], st_ref[...]
    spectra = []
    for signal in range(2 * channels):
        piece = split3(x_ref[signal])
        a_re = dot3(c1, piece)
        a_im = -dot3(s1, piece)
        t_re = split3(a_re * ct + a_im * st)
        t_im = split3(a_im * ct - a_re * st)
        spectra.append((dot3(t_re, c2) + dot3(t_im, s2), dot3(t_im, c2) - dot3(t_re, s2)))
    c1t, s1t = (c1th[...], c1tl[...]), (s1th[...], s1tl[...])
    for channel in range(channels):
        (x_re, x_im), (h_re, h_im) = spectra[channel], spectra[channels + channel]
        p_re = split3(x_re * h_re - x_im * h_im)
        p_im = split3(x_re * h_im + x_im * h_re)
        q_re = dot3(p_re, c2) - dot3(p_im, s2)
        q_im = dot3(p_im, c2) + dot3(p_re, s2)
        u_re = split3(q_re * ct - q_im * st)
        u_im = split3(q_im * ct + q_re * st)
        o_ref[channel] = (dot3(c1t, u_re) - dot3(s1t, u_im)) * scale


def spectral_conv(series, filters):
    channels, seq_length = series.shape
    half = seq_length // BLOCK
    rows = 2 * half
    stacked = jnp.concatenate([series, filters]).reshape(2 * channels, half, BLOCK)
    tables = dft_tables(seq_length)
    signal_flops = 3 * 2 * (2 * rows * half * BLOCK + 4 * rows * BLOCK * BLOCK)
    out = pl.pallas_call(
        conv_kernel,
        out_shape=jax.ShapeDtypeStruct((channels, half, BLOCK), jnp.float32),
        compiler_params=pltpu.CompilerParams(vmem_limit_bytes=100 * 1024 * 1024),
        cost_estimate=pl.CostEstimate(
            flops=3 * channels * signal_flops,
            transcendentals=0,
            bytes_accessed=(3 * channels * half * BLOCK + 6 * rows * BLOCK) * 4,
        ),
        interpret=INTERPRET,
    )(stacked, *tables)
    return out.reshape(channels, seq_length)


def whole_conv(key_value, long_filter):
    joined = jnp.stack([key_value, long_filter])
    regrouped = lax.all_to_all(joined, ("sx", "sc"), split_axis=1, concat_axis=2, tiled=True)
    series = spectral_conv(regrouped[0], regrouped[1])
    return lax.all_to_all(series, ("sx", "sc"), split_axis=1, concat_axis=0, tiled=True)


def shift(value, axis, by):
    count = lax.axis_size(axis)
    return lax.ppermute(value, axis, [(i, (i + by) % count) for i in range(count)])


def ring_gather(piece, axis, split_axis):
    count = lax.axis_size(axis)
    ahead, behind = [piece], [piece]
    for _ in range((count - 1) // 2):
        ahead.append(shift(ahead[-1], axis, -1))
        behind.append(shift(behind[-1], axis, 1))
    order = ahead
    if count % 2 == 0:
        cut = piece.shape[split_axis] // 2
        low = shift(lax.slice_in_dim(behind[-1], 0, cut, axis=split_axis), axis, 1)
        high = shift(lax.slice_in_dim(ahead[-1], cut, None, axis=split_axis), axis, -1)
        order = order + [jnp.concatenate([low, high], axis=split_axis)]
    order = order + behind[1:][::-1]
    return jnp.stack(order)


def rolled_weight(output_weight, first, second):
    rows = output_weight.shape[0]
    size_y, size_z = lax.axis_size("cy"), lax.axis_size("cz")
    grid = output_weight.reshape(rows, size_y, size_z, -1)
    grid = jnp.roll(grid, -lax.axis_index("cy"), axis=1)
    grid = jnp.roll(grid, -lax.axis_index("cz"), axis=2)
    if first == "cy":
        grid = jnp.swapaxes(grid, 1, 2)
    return grid.reshape(rows, -1)


def project(gated, output_weight):
    positions = gated.shape[1]
    cut = positions * 9 // 16
    results = []
    for first, second, part in (("cz", "cy", gated[:, :cut]), ("cy", "cz", gated[:, cut:])):
        inner = ring_gather(part, first, 1)
        outer = ring_gather(inner, second, 2)
        stacked = outer.reshape(-1, part.shape[1])
        weight = rolled_weight(output_weight, first, second)
        results.append(jnp.dot(weight, stacked, preferred_element_type=jnp.float32))
    return jnp.concatenate(results, axis=1).astype(jnp.bfloat16)


def shards(query_input, key_input, value_input, short_taps, long_filter, skip_gain, output_weight):
    channels, positions = query_input.shape
    stacked = jnp.stack([query_input, key_input, value_input])
    before = from_behind(stacked[:, :, positions - 2 :], ("sx", "sc"), 1)
    extended = jnp.concatenate([before, stacked], axis=2).astype(jnp.float32)
    featured = (
        short_taps[0][:, :, None] * extended[:, :, 2:]
        + short_taps[1][:, :, None] * extended[:, :, 1:-1]
        + short_taps[2][:, :, None] * extended[:, :, :-2]
    )
    query_part = featured[0]
    key_value = featured[1] * featured[2]
    convolved = whole_conv(key_value, long_filter)
    gated = (query_part * (convolved + skip_gain[:, None] * key_value)).astype(jnp.bfloat16)
    return project(gated, output_weight)


def solution(mesh):
    seq_size, chan_size = mesh.devices.shape
    z_size = 8 if chan_size % 8 == 0 else chan_size
    grid = Mesh(
        mesh.devices.reshape(seq_size // 2, 2, chan_size // z_size, z_size),
        ("sx", "sc", "cy", "cz"),
    )
    seq = ("sx", "sc")
    chan = ("cy", "cz")
    return jax.shard_map(
        shards,
        mesh=grid,
        in_specs=(
            P(chan, seq),
            P(chan, seq),
            P(chan, seq),
            P(None, None, chan),
            P(chan, seq),
            P(chan),
            P(chan, None),
        ),
        out_specs=P(chan, seq),
        check_vma=False,
    )
```

```python
import numpy as np

import jax
import jax.numpy as jnp
from jax.experimental import pallas as pl
from jax.experimental.pallas import tpu as pltpu
from jax import lax
from jax.sharding import Mesh, PartitionSpec as P

INTERPRET = False
BLOCK = 256


def from_behind(value, axis, by):
    count = lax.axis_size(axis)
    pairs = [(i, i + by) for i in range(count) if 0 <= i + by < count]
    return lax.ppermute(value, axis, pairs)


def dft_tables(seq_length):
    rows = 2 * seq_length // BLOCK
    half = seq_length // BLOCK
    k1 = np.arange(rows)[:, None]
    n1 = np.arange(half)[None, :]
    col = np.arange(BLOCK)
    first = 2.0 * np.pi * ((k1 * n1) % rows) / rows
    second = 2.0 * np.pi * ((col[:, None] * col[None, :]) % BLOCK) / BLOCK
    turn = 2.0 * np.pi * (k1 * col[None, :]) / (2 * seq_length)

    def halves(table):
        table = np.asarray(table, np.float32)
        high = table.astype(jnp.bfloat16)
        low = (table - high.astype(np.float32)).astype(jnp.bfloat16)
        return [jnp.asarray(high), jnp.asarray(low)]

    tables = []
    for table in (np.cos(first), np.sin(first), np.cos(second), np.sin(second), np.cos(first).T, np.sin(first).T):
        tables += halves(table)
    tables += [jnp.asarray(np.cos(turn), jnp.float32), jnp.asarray(np.sin(turn), jnp.float32)]
    return tables


def split3(value):
    high = value.astype(jnp.bfloat16)
    return high, (value - high.astype(jnp.float32)).astype(jnp.bfloat16)


def dot3(a, b):
    def one(p, q):
        return jnp.dot(p, q, preferred_element_type=jnp.float32)

    return one(a[0], b[0]) + (one(a[0], b[1]) + one(a[1], b[0]))


def conv_kernel(x_ref, c1h, c1l, s1h, s1l, c2h, c2l, s2h, s2l, c1th, c1tl, s1th, s1tl, ct_ref, st_ref, o_ref):
    channels = o_ref.shape[0]
    scale = 1.0 / (2 * x_ref.shape[1] * x_ref.shape[2])
    c1, s1 = (c1h[...], c1l[...]), (s1h[...], s1l[...])
    c2, s2 = (c2h[...], c2l[...]), (s2h[...], s2l[...])
    ct, st = ct_ref[...], st_ref[...]
    spectra = []
    for signal in range(2 * channels):
        piece = split3(x_ref[signal])
        a_re = dot3(c1, piece)
        a_im = -dot3(s1, piece)
        t_re = split3(a_re * ct + a_im * st)
        t_im = split3(a_im * ct - a_re * st)
        spectra.append((dot3(t_re, c2) + dot3(t_im, s2), dot3(t_im, c2) - dot3(t_re, s2)))
    c1t, s1t = (c1th[...], c1tl[...]), (s1th[...], s1tl[...])
    for channel in range(channels):
        (x_re, x_im), (h_re, h_im) = spectra[channel], spectra[channels + channel]
        p_re = split3(x_re * h_re - x_im * h_im)
        p_im = split3(x_re * h_im + x_im * h_re)
        q_re = dot3(p_re, c2) - dot3(p_im, s2)
        q_im = dot3(p_im, c2) + dot3(p_re, s2)
        u_re = split3(q_re * ct - q_im * st)
        u_im = split3(q_im * ct + q_re * st)
        o_ref[channel] = (dot3(c1t, u_re) - dot3(s1t, u_im)) * scale


def spectral_conv(series, filters):
    channels, seq_length = series.shape
    half = seq_length // BLOCK
    rows = 2 * half
    stacked = jnp.concatenate([series, filters]).reshape(2 * channels, half, BLOCK)
    tables = dft_tables(seq_length)
    signal_flops = 3 * 2 * (2 * rows * half * BLOCK + 4 * rows * BLOCK * BLOCK)
    out = pl.pallas_call(
        conv_kernel,
        out_shape=jax.ShapeDtypeStruct((channels, half, BLOCK), jnp.float32),
        compiler_params=pltpu.CompilerParams(vmem_limit_bytes=100 * 1024 * 1024),
        cost_estimate=pl.CostEstimate(
            flops=3 * channels * signal_flops,
            transcendentals=0,
            bytes_accessed=(3 * channels * half * BLOCK + 6 * rows * BLOCK) * 4,
        ),
        interpret=INTERPRET,
    )(stacked, *tables)
    return out.reshape(channels, seq_length)


def whole_conv(key_value, long_filter):
    joined = jnp.stack([key_value, long_filter])
    regrouped = lax.all_to_all(joined, ("sx", "sc"), split_axis=1, concat_axis=2, tiled=True)
    series = spectral_conv(regrouped[0], regrouped[1])
    return lax.all_to_all(series, ("sx", "sc"), split_axis=1, concat_axis=0, tiled=True)


def shift(value, axis, by):
    count = lax.axis_size(axis)
    return lax.ppermute(value, axis, [(i, (i + by) % count) for i in range(count)])


def ring_gather(piece, axis, split_axis):
    count = lax.axis_size(axis)
    ahead, behind = [piece], [piece]
    for _ in range((count - 1) // 2):
        ahead.append(shift(ahead[-1], axis, -1))
        behind.append(shift(behind[-1], axis, 1))
    order = ahead
    if count % 2 == 0:
        cut = piece.shape[split_axis] // 2
        low = shift(lax.slice_in_dim(behind[-1], 0, cut, axis=split_axis), axis, 1)
        high = shift(lax.slice_in_dim(ahead[-1], cut, None, axis=split_axis), axis, -1)
        order = order + [jnp.concatenate([low, high], axis=split_axis)]
    order = order + behind[1:][::-1]
    return jnp.stack(order)


def rolled_weight(output_weight, first, second):
    rows = output_weight.shape[0]
    size_y, size_z = lax.axis_size("cy"), lax.axis_size("cz")
    grid = output_weight.reshape(rows, size_y, size_z, -1)
    grid = jnp.roll(grid, -lax.axis_index("cy"), axis=1)
    grid = jnp.roll(grid, -lax.axis_index("cz"), axis=2)
    if first == "cy":
        grid = jnp.swapaxes(grid, 1, 2)
    return grid.reshape(rows, -1)


def project(gated, output_weight):
    positions = gated.shape[1]
    cut = positions * 9 // 16
    gathered = lax.all_gather(gated[:, cut:], ("cy", "cz"), axis=0, tiled=True)
    inner = ring_gather(gated[:, :cut], "cz", 1)
    outer = ring_gather(inner, "cy", 2)
    stacked = outer.reshape(-1, cut)
    weight = rolled_weight(output_weight, "cz", "cy")
    results = [
        jnp.dot(weight, stacked, preferred_element_type=jnp.float32),
        jnp.dot(output_weight, gathered, preferred_element_type=jnp.float32),
    ]
    return jnp.concatenate(results, axis=1).astype(jnp.bfloat16)


def shards(query_input, key_input, value_input, short_taps, long_filter, skip_gain, output_weight):
    channels, positions = query_input.shape
    stacked = jnp.stack([query_input, key_input, value_input])
    before = from_behind(stacked[:, :, positions - 2 :], ("sx", "sc"), 1)
    extended = jnp.concatenate([before, stacked], axis=2).astype(jnp.float32)
    featured = (
        short_taps[0][:, :, None] * extended[:, :, 2:]
        + short_taps[1][:, :, None] * extended[:, :, 1:-1]
        + short_taps[2][:, :, None] * extended[:, :, :-2]
    )
    query_part = featured[0]
    key_value = featured[1] * featured[2]
    convolved = whole_conv(key_value, long_filter)
    gated = (query_part * (convolved + skip_gain[:, None] * key_value)).astype(jnp.bfloat16)
    return project(gated, output_weight)


def solution(mesh):
    seq_size, chan_size = mesh.devices.shape
    z_size = 8 if chan_size % 8 == 0 else chan_size
    grid = Mesh(
        mesh.devices.reshape(seq_size // 2, 2, chan_size // z_size, z_size),
        ("sx", "sc", "cy", "cz"),
    )
    seq = ("sx", "sc")
    chan = ("cy", "cz")
    return jax.shard_map(
        shards,
        mesh=grid,
        in_specs=(
            P(chan, seq),
            P(chan, seq),
            P(chan, seq),
            P(None, None, chan),
            P(chan, seq),
            P(chan),
            P(chan, None),
        ),
        out_specs=P(chan, seq),
        check_vma=False,
    )
```

```python
import numpy as np

import jax
import jax.numpy as jnp
from jax.experimental import pallas as pl
from jax.experimental.pallas import tpu as pltpu
from jax import lax
from jax.sharding import Mesh, PartitionSpec as P

INTERPRET = False
BLOCK = 256


def from_behind(value, axis, by):
    count = lax.axis_size(axis)
    pairs = [(i, i + by) for i in range(count) if 0 <= i + by < count]
    return lax.ppermute(value, axis, pairs)


def dft_tables(seq_length):
    rows = 2 * seq_length // BLOCK
    half = seq_length // BLOCK
    k1 = np.arange(rows)[:, None]
    n1 = np.arange(half)[None, :]
    col = np.arange(BLOCK)
    first = 2.0 * np.pi * ((k1 * n1) % rows) / rows
    second = 2.0 * np.pi * ((col[:, None] * col[None, :]) % BLOCK) / BLOCK
    turn = 2.0 * np.pi * (k1 * col[None, :]) / (2 * seq_length)

    def halves(table):
        table = np.asarray(table, np.float32)
        high = table.astype(jnp.bfloat16)
        low = (table - high.astype(np.float32)).astype(jnp.bfloat16)
        return [jnp.asarray(high), jnp.asarray(low)]

    tables = []
    for table in (np.cos(first), np.sin(first), np.cos(second), np.sin(second), np.cos(first).T, np.sin(first).T):
        tables += halves(table)
    tables += [jnp.asarray(np.cos(turn), jnp.float32), jnp.asarray(np.sin(turn), jnp.float32)]
    return tables


def split3(value):
    high = value.astype(jnp.bfloat16)
    return high, (value - high.astype(jnp.float32)).astype(jnp.bfloat16)


def dot3(a, b):
    def one(p, q):
        return jnp.dot(p, q, preferred_element_type=jnp.float32)

    return one(a[0], b[0]) + (one(a[0], b[1]) + one(a[1], b[0]))


def conv_kernel(x_ref, c1h, c1l, s1h, s1l, c2h, c2l, s2h, s2l, c1th, c1tl, s1th, s1tl, ct_ref, st_ref, o_ref):
    channels = o_ref.shape[0]
    scale = 1.0 / (2 * x_ref.shape[1] * x_ref.shape[2])
    c1, s1 = (c1h[...], c1l[...]), (s1h[...], s1l[...])
    c2, s2 = (c2h[...], c2l[...]), (s2h[...], s2l[...])
    ct, st = ct_ref[...], st_ref[...]
    spectra = []
    for signal in range(2 * channels):
        piece = split3(x_ref[signal])
        a_re = dot3(c1, piece)
        a_im = -dot3(s1, piece)
        t_re = split3(a_re * ct + a_im * st)
        t_im = split3(a_im * ct - a_re * st)
        spectra.append((dot3(t_re, c2) + dot3(t_im, s2), dot3(t_im, c2) - dot3(t_re, s2)))
    c1t, s1t = (c1th[...], c1tl[...]), (s1th[...], s1tl[...])
    for channel in range(channels):
        (x_re, x_im), (h_re, h_im) = spectra[channel], spectra[channels + channel]
        p_re = split3(x_re * h_re - x_im * h_im)
        p_im = split3(x_re * h_im + x_im * h_re)
        q_re = dot3(p_re, c2) - dot3(p_im, s2)
        q_im = dot3(p_im, c2) + dot3(p_re, s2)
        u_re = split3(q_re * ct - q_im * st)
        u_im = split3(q_im * ct + q_re * st)
        o_ref[channel] = (dot3(c1t, u_re) - dot3(s1t, u_im)) * scale


def spectral_conv(series, filters):
    channels, seq_length = series.shape
    half = seq_length // BLOCK
    rows = 2 * half
    stacked = jnp.concatenate([series, filters]).reshape(2 * channels, half, BLOCK)
    tables = dft_tables(seq_length)
    signal_flops = 3 * 2 * (2 * rows * half * BLOCK + 4 * rows * BLOCK * BLOCK)
    out = pl.pallas_call(
        conv_kernel,
        out_shape=jax.ShapeDtypeStruct((channels, half, BLOCK), jnp.float32),
        compiler_params=pltpu.CompilerParams(vmem_limit_bytes=100 * 1024 * 1024),
        cost_estimate=pl.CostEstimate(
            flops=3 * channels * signal_flops,
            transcendentals=0,
            bytes_accessed=(3 * channels * half * BLOCK + 6 * rows * BLOCK) * 4,
        ),
        interpret=INTERPRET,
    )(stacked, *tables)
    return out.reshape(channels, seq_length)


def whole_conv(key_value, long_filter):
    joined = jnp.stack([key_value, long_filter])
    regrouped = lax.all_to_all(joined, ("sx", "sc"), split_axis=1, concat_axis=2, tiled=True)
    series = spectral_conv(regrouped[0], regrouped[1])
    return lax.all_to_all(series, ("sx", "sc"), split_axis=1, concat_axis=0, tiled=True)


def shift(value, axis, by):
    count = lax.axis_size(axis)
    return lax.ppermute(value, axis, [(i, (i + by) % count) for i in range(count)])


def ring_gather(piece, axis, split_axis):
    count = lax.axis_size(axis)
    ahead, behind = [piece], [piece]
    for _ in range((count - 1) // 2):
        ahead.append(shift(ahead[-1], axis, -1))
        behind.append(shift(behind[-1], axis, 1))
    order = ahead
    if count % 2 == 0:
        cut = piece.shape[split_axis] // 2
        low = shift(lax.slice_in_dim(behind[-1], 0, cut, axis=split_axis), axis, 1)
        high = shift(lax.slice_in_dim(ahead[-1], cut, None, axis=split_axis), axis, -1)
        order = order + [jnp.concatenate([low, high], axis=split_axis)]
    order = order + behind[1:][::-1]
    return jnp.stack(order)


def rolled_weight(output_weight, first, second):
    rows = output_weight.shape[0]
    size_y, size_z = lax.axis_size("cy"), lax.axis_size("cz")
    grid = output_weight.reshape(rows, size_y, size_z, -1)
    grid = jnp.roll(grid, -lax.axis_index("cy"), axis=1)
    grid = jnp.roll(grid, -lax.axis_index("cz"), axis=2)
    if first == "cy":
        grid = jnp.swapaxes(grid, 1, 2)
    return grid.reshape(rows, -1)


def project(gated, output_weight):
    positions = gated.shape[1]
    cut = positions * 9 // 16
    results = []
    for first, second, part in (("cz", "cy", gated[:, :cut]), ("cy", "cz", gated[:, cut:])):
        inner = ring_gather(part, first, 1)
        outer = ring_gather(inner, second, 2)
        stacked = outer.reshape(-1, part.shape[1])
        weight = rolled_weight(output_weight, first, second)
        results.append(jnp.dot(weight, stacked, preferred_element_type=jnp.float32))
    return jnp.concatenate(results, axis=1)


def shards(query_input, key_input, value_input, short_taps, long_filter, skip_gain, output_weight):
    channels, positions = query_input.shape
    stacked = jnp.stack([query_input, key_input, value_input])
    before = from_behind(stacked[:, :, positions - 2 :], ("sx", "sc"), 1)
    extended = jnp.concatenate([before, stacked], axis=2).astype(jnp.float32)
    featured = (
        short_taps[0][:, :, None] * extended[:, :, 2:]
        + short_taps[1][:, :, None] * extended[:, :, 1:-1]
        + short_taps[2][:, :, None] * extended[:, :, :-2]
    )
    query_part = featured[0]
    key_value = featured[1] * featured[2]
    rows = output_weight.shape[0]
    groups = 2
    per = channels // groups
    total = None
    previous = None
    for group in range(groups):
        part = slice(group * per, (group + 1) * per)
        series, filters = key_value[part], long_filter[part]
        if previous is not None:
            previous, series, filters = lax.optimization_barrier((previous, series, filters))
        convolved = whole_conv(series, filters)
        gated = (query_part[part] * (convolved + skip_gain[part, None] * key_value[part])).astype(jnp.bfloat16)
        weight = output_weight.reshape(rows, -1, channels)[:, :, part].reshape(rows, -1)
        if group == 0:
            previous = gated
            gathered = lax.all_gather(gated, ("cy", "cz"), axis=0, tiled=True)
            term = jnp.dot(weight, gathered, preferred_element_type=jnp.float32)
        else:
            term = project(gated, weight)
        total = term if total is None else total + term
    return total.astype(jnp.bfloat16)


def solution(mesh):
    seq_size, chan_size = mesh.devices.shape
    z_size = 8 if chan_size % 8 == 0 else chan_size
    grid = Mesh(
        mesh.devices.reshape(seq_size // 2, 2, chan_size // z_size, z_size),
        ("sx", "sc", "cy", "cz"),
    )
    seq = ("sx", "sc")
    chan = ("cy", "cz")
    return jax.shard_map(
        shards,
        mesh=grid,
        in_specs=(
            P(chan, seq),
            P(chan, seq),
            P(chan, seq),
            P(None, None, chan),
            P(chan, seq),
            P(chan),
            P(chan, None),
        ),
        out_specs=P(chan, seq),
        check_vma=False,
    )
```

```python
import numpy as np

import jax
import jax.numpy as jnp
from jax.experimental import pallas as pl
from jax.experimental.pallas import tpu as pltpu
from jax import lax
from jax.sharding import Mesh, PartitionSpec as P

INTERPRET = False
BLOCK = 256


def from_behind(value, axis, by):
    count = lax.axis_size(axis)
    pairs = [(i, i + by) for i in range(count) if 0 <= i + by < count]
    return lax.ppermute(value, axis, pairs)


def dft_tables(seq_length):
    rows = 2 * seq_length // BLOCK
    half = seq_length // BLOCK
    k1 = np.arange(rows)[:, None]
    n1 = np.arange(half)[None, :]
    col = np.arange(BLOCK)
    first = 2.0 * np.pi * ((k1 * n1) % rows) / rows
    second = 2.0 * np.pi * ((col[:, None] * col[None, :]) % BLOCK) / BLOCK
    turn = 2.0 * np.pi * (k1 * col[None, :]) / (2 * seq_length)

    def halves(table):
        table = np.asarray(table, np.float32)
        high = table.astype(jnp.bfloat16)
        low = (table - high.astype(np.float32)).astype(jnp.bfloat16)
        return [jnp.asarray(high), jnp.asarray(low)]

    tables = []
    for table in (np.cos(first), np.sin(first), np.cos(second), np.sin(second), np.cos(first).T, np.sin(first).T):
        tables += halves(table)
    tables += [jnp.asarray(np.cos(turn), jnp.float32), jnp.asarray(np.sin(turn), jnp.float32)]
    return tables


def split3(value):
    high = value.astype(jnp.bfloat16)
    return high, (value - high.astype(jnp.float32)).astype(jnp.bfloat16)


def dot3(a, b):
    def one(p, q):
        return jnp.dot(p, q, preferred_element_type=jnp.float32)

    return one(a[0], b[0]) + (one(a[0], b[1]) + one(a[1], b[0]))


def conv_kernel(x_ref, c1h, c1l, s1h, s1l, c2h, c2l, s2h, s2l, c1th, c1tl, s1th, s1tl, ct_ref, st_ref, o_ref):
    channels = o_ref.shape[0]
    scale = 1.0 / (2 * x_ref.shape[1] * x_ref.shape[2])
    c1, s1 = (c1h[...], c1l[...]), (s1h[...], s1l[...])
    c2, s2 = (c2h[...], c2l[...]), (s2h[...], s2l[...])
    ct, st = ct_ref[...], st_ref[...]
    spectra = []
    for signal in range(2 * channels):
        piece = split3(x_ref[signal])
        a_re = dot3(c1, piece)
        a_im = -dot3(s1, piece)
        t_re = split3(a_re * ct + a_im * st)
        t_im = split3(a_im * ct - a_re * st)
        spectra.append((dot3(t_re, c2) + dot3(t_im, s2), dot3(t_im, c2) - dot3(t_re, s2)))
    c1t, s1t = (c1th[...], c1tl[...]), (s1th[...], s1tl[...])
    for channel in range(channels):
        (x_re, x_im), (h_re, h_im) = spectra[channel], spectra[channels + channel]
        p_re = split3(x_re * h_re - x_im * h_im)
        p_im = split3(x_re * h_im + x_im * h_re)
        q_re = dot3(p_re, c2) - dot3(p_im, s2)
        q_im = dot3(p_im, c2) + dot3(p_re, s2)
        u_re = split3(q_re * ct - q_im * st)
        u_im = split3(q_im * ct + q_re * st)
        o_ref[channel] = (dot3(c1t, u_re) - dot3(s1t, u_im)) * scale


def spectral_conv(series, filters):
    channels, seq_length = series.shape
    half = seq_length // BLOCK
    rows = 2 * half
    stacked = jnp.concatenate([series, filters]).reshape(2 * channels, half, BLOCK)
    tables = dft_tables(seq_length)
    signal_flops = 3 * 2 * (2 * rows * half * BLOCK + 4 * rows * BLOCK * BLOCK)
    out = pl.pallas_call(
        conv_kernel,
        out_shape=jax.ShapeDtypeStruct((channels, half, BLOCK), jnp.float32),
        compiler_params=pltpu.CompilerParams(vmem_limit_bytes=100 * 1024 * 1024),
        cost_estimate=pl.CostEstimate(
            flops=3 * channels * signal_flops,
            transcendentals=0,
            bytes_accessed=(3 * channels * half * BLOCK + 6 * rows * BLOCK) * 4,
        ),
        interpret=INTERPRET,
    )(stacked, *tables)
    return out.reshape(channels, seq_length)


def whole_conv(key_value, long_filter):
    joined = jnp.stack([key_value, long_filter])
    regrouped = lax.all_to_all(joined, ("sx", "sc"), split_axis=1, concat_axis=2, tiled=True)
    series = spectral_conv(regrouped[0], regrouped[1])
    return lax.all_to_all(series, ("sx", "sc"), split_axis=1, concat_axis=0, tiled=True)


def shift(value, axis, by):
    count = lax.axis_size(axis)
    return lax.ppermute(value, axis, [(i, (i + by) % count) for i in range(count)])


def ring_gather(piece, axis, split_axis):
    count = lax.axis_size(axis)
    ahead, behind = [piece], [piece]
    for _ in range((count - 1) // 2):
        ahead.append(shift(ahead[-1], axis, -1))
        behind.append(shift(behind[-1], axis, 1))
    order = ahead
    if count % 2 == 0:
        order = order + [shift(behind[-1], axis, 1)]
    order = order + behind[1:][::-1]
    return jnp.stack(order)


def rolled_weight(output_weight, first, second):
    rows = output_weight.shape[0]
    size_y, size_z = lax.axis_size("cy"), lax.axis_size("cz")
    grid = output_weight.reshape(rows, size_y, size_z, -1)
    grid = jnp.roll(grid, -lax.axis_index("cy"), axis=1)
    grid = jnp.roll(grid, -lax.axis_index("cz"), axis=2)
    if first == "cy":
        grid = jnp.swapaxes(grid, 1, 2)
    return grid.reshape(rows, -1)


def project(gated, output_weight):
    positions = gated.shape[1]
    cut = positions * 9 // 16
    results = []
    for first, second, part in (("cz", "cy", gated[:, :cut]), ("cy", "cz", gated[:, cut:])):
        inner = ring_gather(part, first, 1)
        outer = ring_gather(inner, second, 2)
        stacked = outer.reshape(-1, part.shape[1])
        weight = rolled_weight(output_weight, first, second)
        results.append(jnp.dot(weight, stacked, preferred_element_type=jnp.float32))
    return jnp.concatenate(results, axis=1).astype(jnp.bfloat16)


def shards(query_input, key_input, value_input, short_taps, long_filter, skip_gain, output_weight):
    channels, positions = query_input.shape
    stacked = jnp.stack([query_input, key_input, value_input])
    before = from_behind(stacked[:, :, positions - 2 :], ("sx", "sc"), 1)
    extended = jnp.concatenate([before, stacked], axis=2).astype(jnp.float32)
    featured = (
        short_taps[0][:, :, None] * extended[:, :, 2:]
        + short_taps[1][:, :, None] * extended[:, :, 1:-1]
        + short_taps[2][:, :, None] * extended[:, :, :-2]
    )
    query_part = featured[0]
    key_value = featured[1] * featured[2]
    convolved = whole_conv(key_value, long_filter)
    gated = (query_part * (convolved + skip_gain[:, None] * key_value)).astype(jnp.bfloat16)
    return project(gated, output_weight)


def solution(mesh):
    seq_size, chan_size = mesh.devices.shape
    z_size = 8 if chan_size % 8 == 0 else chan_size
    grid = Mesh(
        mesh.devices.reshape(seq_size // 2, 2, chan_size // z_size, z_size),
        ("sx", "sc", "cy", "cz"),
    )
    seq = ("sx", "sc")
    chan = ("cy", "cz")
    return jax.shard_map(
        shards,
        mesh=grid,
        in_specs=(
            P(chan, seq),
            P(chan, seq),
            P(chan, seq),
            P(None, None, chan),
            P(chan, seq),
            P(chan),
            P(chan, None),
        ),
        out_specs=P(chan, seq),
        check_vma=False,
    )
```

```python
import numpy as np

import jax
import jax.numpy as jnp
from jax.experimental import pallas as pl
from jax.experimental.pallas import tpu as pltpu
from jax import lax
from jax.sharding import Mesh, PartitionSpec as P

INTERPRET = False
BLOCK = 256


def from_behind(value, axis, by):
    count = lax.axis_size(axis)
    pairs = [(i, i + by) for i in range(count) if 0 <= i + by < count]
    return lax.ppermute(value, axis, pairs)


def dft_tables(seq_length):
    rows = 2 * seq_length // BLOCK
    half = seq_length // BLOCK
    k1 = np.arange(rows)[:, None]
    n1 = np.arange(half)[None, :]
    col = np.arange(BLOCK)
    first = 2.0 * np.pi * ((k1 * n1) % rows) / rows
    second = 2.0 * np.pi * ((col[:, None] * col[None, :]) % BLOCK) / BLOCK
    turn = 2.0 * np.pi * (k1 * col[None, :]) / (2 * seq_length)

    def halves(table):
        table = np.asarray(table, np.float32)
        high = table.astype(jnp.bfloat16)
        low = (table - high.astype(np.float32)).astype(jnp.bfloat16)
        return [jnp.asarray(high), jnp.asarray(low)]

    tables = []
    for table in (np.cos(first), np.sin(first), np.cos(second), np.sin(second), np.cos(first).T, np.sin(first).T):
        tables += halves(table)
    tables += [jnp.asarray(np.cos(turn), jnp.float32), jnp.asarray(np.sin(turn), jnp.float32)]
    return tables


def split3(value):
    high = value.astype(jnp.bfloat16)
    return high, (value - high.astype(jnp.float32)).astype(jnp.bfloat16)


def dot3(a, b):
    def one(p, q):
        return jnp.dot(p, q, preferred_element_type=jnp.float32)

    return one(a[0], b[0]) + (one(a[0], b[1]) + one(a[1], b[0]))


def conv_kernel(x_ref, c1h, c1l, s1h, s1l, c2h, c2l, s2h, s2l, c1th, c1tl, s1th, s1tl, ct_ref, st_ref, o_ref):
    channels = o_ref.shape[0]
    scale = 1.0 / (2 * x_ref.shape[1] * x_ref.shape[2])
    c1, s1 = (c1h[...], c1l[...]), (s1h[...], s1l[...])
    c2, s2 = (c2h[...], c2l[...]), (s2h[...], s2l[...])
    ct, st = ct_ref[...], st_ref[...]
    spectra = []
    for signal in range(2 * channels):
        piece = split3(x_ref[signal])
        a_re = dot3(c1, piece)
        a_im = -dot3(s1, piece)
        t_re = split3(a_re * ct + a_im * st)
        t_im = split3(a_im * ct - a_re * st)
        spectra.append((dot3(t_re, c2) + dot3(t_im, s2), dot3(t_im, c2) - dot3(t_re, s2)))
    c1t, s1t = (c1th[...], c1tl[...]), (s1th[...], s1tl[...])
    for channel in range(channels):
        (x_re, x_im), (h_re, h_im) = spectra[channel], spectra[channels + channel]
        p_re = split3(x_re * h_re - x_im * h_im)
        p_im = split3(x_re * h_im + x_im * h_re)
        q_re = dot3(p_re, c2) - dot3(p_im, s2)
        q_im = dot3(p_im, c2) + dot3(p_re, s2)
        u_re = split3(q_re * ct - q_im * st)
        u_im = split3(q_im * ct + q_re * st)
        o_ref[channel] = (dot3(c1t, u_re) - dot3(s1t, u_im)) * scale


def spectral_conv(series, filters):
    channels, seq_length = series.shape
    half = seq_length // BLOCK
    rows = 2 * half
    stacked = jnp.concatenate([series, filters]).reshape(2 * channels, half, BLOCK)
    tables = dft_tables(seq_length)
    signal_flops = 3 * 2 * (2 * rows * half * BLOCK + 4 * rows * BLOCK * BLOCK)
    out = pl.pallas_call(
        conv_kernel,
        out_shape=jax.ShapeDtypeStruct((channels, half, BLOCK), jnp.float32),
        compiler_params=pltpu.CompilerParams(vmem_limit_bytes=100 * 1024 * 1024),
        cost_estimate=pl.CostEstimate(
            flops=3 * channels * signal_flops,
            transcendentals=0,
            bytes_accessed=(3 * channels * half * BLOCK + 6 * rows * BLOCK) * 4,
        ),
        interpret=INTERPRET,
    )(stacked, *tables)
    return out.reshape(channels, seq_length)


def whole_conv(key_value, long_filter):
    filters = lax.all_to_all(long_filter, ("sx", "sc"), split_axis=0, concat_axis=1, tiled=True)
    products = lax.all_to_all(key_value, ("sx", "sc"), split_axis=0, concat_axis=1, tiled=True)
    series = spectral_conv(products, filters)
    return lax.all_to_all(series, ("sx", "sc"), split_axis=1, concat_axis=0, tiled=True)


def shift(value, axis, by):
    count = lax.axis_size(axis)
    return lax.ppermute(value, axis, [(i, (i + by) % count) for i in range(count)])


def ring_gather(piece, axis, split_axis):
    count = lax.axis_size(axis)
    ahead, behind = [piece], [piece]
    for _ in range((count - 1) // 2):
        ahead.append(shift(ahead[-1], axis, -1))
        behind.append(shift(behind[-1], axis, 1))
    order = ahead
    if count % 2 == 0:
        cut = piece.shape[split_axis] // 2
        low = shift(lax.slice_in_dim(behind[-1], 0, cut, axis=split_axis), axis, 1)
        high = shift(lax.slice_in_dim(ahead[-1], cut, None, axis=split_axis), axis, -1)
        order = order + [jnp.concatenate([low, high], axis=split_axis)]
    order = order + behind[1:][::-1]
    return jnp.stack(order)


def rolled_weight(output_weight, first, second):
    rows = output_weight.shape[0]
    size_y, size_z = lax.axis_size("cy"), lax.axis_size("cz")
    grid = output_weight.reshape(rows, size_y, size_z, -1)
    grid = jnp.roll(grid, -lax.axis_index("cy"), axis=1)
    grid = jnp.roll(grid, -lax.axis_index("cz"), axis=2)
    if first == "cy":
        grid = jnp.swapaxes(grid, 1, 2)
    return grid.reshape(rows, -1)


def project(gated, output_weight):
    positions = gated.shape[1]
    cut = positions * 9 // 16
    results = []
    for first, second, part in (("cz", "cy", gated[:, :cut]), ("cy", "cz", gated[:, cut:])):
        inner = ring_gather(part, first, 1)
        outer = ring_gather(inner, second, 2)
        stacked = outer.reshape(-1, part.shape[1])
        weight = rolled_weight(output_weight, first, second)
        results.append(jnp.dot(weight, stacked, preferred_element_type=jnp.float32))
    return jnp.concatenate(results, axis=1).astype(jnp.bfloat16)


def shards(query_input, key_input, value_input, short_taps, long_filter, skip_gain, output_weight):
    channels, positions = query_input.shape
    stacked = jnp.stack([query_input, key_input, value_input])
    before = from_behind(stacked[:, :, positions - 2 :], ("sx", "sc"), 1)
    extended = jnp.concatenate([before, stacked], axis=2).astype(jnp.float32)
    featured = (
        short_taps[0][:, :, None] * extended[:, :, 2:]
        + short_taps[1][:, :, None] * extended[:, :, 1:-1]
        + short_taps[2][:, :, None] * extended[:, :, :-2]
    )
    query_part = featured[0]
    key_value = featured[1] * featured[2]
    convolved = whole_conv(key_value, long_filter)
    gated = (query_part * (convolved + skip_gain[:, None] * key_value)).astype(jnp.bfloat16)
    return project(gated, output_weight)


def solution(mesh):
    seq_size, chan_size = mesh.devices.shape
    z_size = 8 if chan_size % 8 == 0 else chan_size
    grid = Mesh(
        mesh.devices.reshape(seq_size // 2, 2, chan_size // z_size, z_size),
        ("sx", "sc", "cy", "cz"),
    )
    seq = ("sx", "sc")
    chan = ("cy", "cz")
    return jax.shard_map(
        shards,
        mesh=grid,
        in_specs=(
            P(chan, seq),
            P(chan, seq),
            P(chan, seq),
            P(None, None, chan),
            P(chan, seq),
            P(chan),
            P(chan, None),
        ),
        out_specs=P(chan, seq),
        check_vma=False,
    )
```

```python
import numpy as np

import jax
import jax.numpy as jnp
from jax.experimental import pallas as pl
from jax.experimental.pallas import tpu as pltpu
from jax import lax
from jax.sharding import Mesh, PartitionSpec as P

INTERPRET = False
BLOCK = 256


def from_behind(value, axis, by):
    count = lax.axis_size(axis)
    pairs = [(i, i + by) for i in range(count) if 0 <= i + by < count]
    return lax.ppermute(value, axis, pairs)


def dft_tables(seq_length):
    rows = 2 * seq_length // BLOCK
    half = seq_length // BLOCK
    k1 = np.arange(rows)[:, None]
    n1 = np.arange(half)[None, :]
    col = np.arange(BLOCK)
    first = 2.0 * np.pi * ((k1 * n1) % rows) / rows
    second = 2.0 * np.pi * ((col[:, None] * col[None, :]) % BLOCK) / BLOCK
    turn = 2.0 * np.pi * (k1 * col[None, :]) / (2 * seq_length)

    def halves(table):
        table = np.asarray(table, np.float32)
        high = table.astype(jnp.bfloat16)
        low = (table - high.astype(np.float32)).astype(jnp.bfloat16)
        return [jnp.asarray(high), jnp.asarray(low)]

    tables = []
    for table in (np.cos(first), np.sin(first), np.cos(second), np.sin(second), np.cos(first).T, np.sin(first).T):
        tables += halves(table)
    tables += [jnp.asarray(np.cos(turn), jnp.float32), jnp.asarray(np.sin(turn), jnp.float32)]
    return tables


def split3(value):
    high = value.astype(jnp.bfloat16)
    return high, (value - high.astype(jnp.float32)).astype(jnp.bfloat16)


def dot3(a, b):
    def one(p, q):
        return jnp.dot(p, q, preferred_element_type=jnp.float32)

    return one(a[0], b[0]) + (one(a[0], b[1]) + one(a[1], b[0]))


def conv_kernel(x_ref, c1h, c1l, s1h, s1l, c2h, c2l, s2h, s2l, c1th, c1tl, s1th, s1tl, ct_ref, st_ref, o_ref):
    channels = o_ref.shape[0]
    scale = 1.0 / (2 * x_ref.shape[1] * x_ref.shape[2])
    c1, s1 = (c1h[...], c1l[...]), (s1h[...], s1l[...])
    c2, s2 = (c2h[...], c2l[...]), (s2h[...], s2l[...])
    ct, st = ct_ref[...], st_ref[...]
    spectra = []
    for signal in range(2 * channels):
        piece = split3(x_ref[signal])
        a_re = dot3(c1, piece)
        a_im = -dot3(s1, piece)
        t_re = split3(a_re * ct + a_im * st)
        t_im = split3(a_im * ct - a_re * st)
        spectra.append((dot3(t_re, c2) + dot3(t_im, s2), dot3(t_im, c2) - dot3(t_re, s2)))
    c1t, s1t = (c1th[...], c1tl[...]), (s1th[...], s1tl[...])
    for channel in range(channels):
        (x_re, x_im), (h_re, h_im) = spectra[channel], spectra[channels + channel]
        p_re = split3(x_re * h_re - x_im * h_im)
        p_im = split3(x_re * h_im + x_im * h_re)
        q_re = dot3(p_re, c2) - dot3(p_im, s2)
        q_im = dot3(p_im, c2) + dot3(p_re, s2)
        u_re = split3(q_re * ct - q_im * st)
        u_im = split3(q_im * ct + q_re * st)
        o_ref[channel] = (dot3(c1t, u_re) - dot3(s1t, u_im)) * scale


def spectral_conv(series, filters):
    channels, seq_length = series.shape
    half = seq_length // BLOCK
    rows = 2 * half
    stacked = jnp.concatenate([series, filters]).reshape(2 * channels, half, BLOCK)
    tables = dft_tables(seq_length)
    signal_flops = 3 * 2 * (2 * rows * half * BLOCK + 4 * rows * BLOCK * BLOCK)
    out = pl.pallas_call(
        conv_kernel,
        out_shape=jax.ShapeDtypeStruct((channels, half, BLOCK), jnp.float32),
        compiler_params=pltpu.CompilerParams(vmem_limit_bytes=100 * 1024 * 1024),
        cost_estimate=pl.CostEstimate(
            flops=3 * channels * signal_flops,
            transcendentals=0,
            bytes_accessed=(3 * channels * half * BLOCK + 6 * rows * BLOCK) * 4,
        ),
        interpret=INTERPRET,
    )(stacked, *tables)
    return out.reshape(channels, seq_length)


def whole_conv(key_value, long_filter):
    joined = jnp.stack([key_value, long_filter])
    regrouped = lax.all_to_all(joined, ("sx", "sc"), split_axis=1, concat_axis=2, tiled=True)
    series = spectral_conv(regrouped[0], regrouped[1])
    return lax.all_to_all(series, ("sx", "sc"), split_axis=1, concat_axis=0, tiled=True)


def shift(value, axis, by):
    count = lax.axis_size(axis)
    return lax.ppermute(value, axis, [(i, (i + by) % count) for i in range(count)])


def ring_gather(piece, axis, split_axis):
    count = lax.axis_size(axis)
    ahead, behind = [piece], [piece]
    for _ in range((count - 1) // 2):
        ahead.append(shift(ahead[-1], axis, -1))
        behind.append(shift(behind[-1], axis, 1))
    order = ahead
    if count % 2 == 0:
        cut = piece.shape[split_axis] // 2
        low = shift(lax.slice_in_dim(behind[-1], 0, cut, axis=split_axis), axis, 1)
        high = shift(lax.slice_in_dim(ahead[-1], cut, None, axis=split_axis), axis, -1)
        order = order + [jnp.concatenate([low, high], axis=split_axis)]
    order = order + behind[1:][::-1]
    return jnp.stack(order)


def rolled_weight(output_weight, first, second):
    rows = output_weight.shape[0]
    size_y, size_z = lax.axis_size("cy"), lax.axis_size("cz")
    grid = output_weight.reshape(rows, size_y, size_z, -1)
    grid = jnp.roll(grid, -lax.axis_index("cy"), axis=1)
    grid = jnp.roll(grid, -lax.axis_index("cz"), axis=2)
    if first == "cy":
        grid = jnp.swapaxes(grid, 1, 2)
    return grid.reshape(rows, -1)


def project(gated, output_weight):
    positions = gated.shape[1]
    cut = positions * 7 // 16
    rest = positions * 3 // 4
    gathered = lax.all_gather(gated[:, rest:], ("cy", "cz"), axis=0, tiled=True)
    results = []
    for first, second, part in (("cz", "cy", gated[:, :cut]), ("cy", "cz", gated[:, cut:rest])):
        inner = ring_gather(part, first, 1)
        outer = ring_gather(inner, second, 2)
        stacked = outer.reshape(-1, part.shape[1])
        weight = rolled_weight(output_weight, first, second)
        results.append(jnp.dot(weight, stacked, preferred_element_type=jnp.float32))
    results.append(jnp.dot(output_weight, gathered, preferred_element_type=jnp.float32))
    return jnp.concatenate(results, axis=1).astype(jnp.bfloat16)


def shards(query_input, key_input, value_input, short_taps, long_filter, skip_gain, output_weight):
    channels, positions = query_input.shape
    stacked = jnp.stack([query_input, key_input, value_input])
    before = from_behind(stacked[:, :, positions - 2 :], ("sx", "sc"), 1)
    extended = jnp.concatenate([before, stacked], axis=2).astype(jnp.float32)
    featured = (
        short_taps[0][:, :, None] * extended[:, :, 2:]
        + short_taps[1][:, :, None] * extended[:, :, 1:-1]
        + short_taps[2][:, :, None] * extended[:, :, :-2]
    )
    query_part = featured[0]
    key_value = featured[1] * featured[2]
    convolved = whole_conv(key_value, long_filter)
    gated = (query_part * (convolved + skip_gain[:, None] * key_value)).astype(jnp.bfloat16)
    return project(gated, output_weight)


def solution(mesh):
    seq_size, chan_size = mesh.devices.shape
    z_size = 8 if chan_size % 8 == 0 else chan_size
    grid = Mesh(
        mesh.devices.reshape(seq_size // 2, 2, chan_size // z_size, z_size),
        ("sx", "sc", "cy", "cz"),
    )
    seq = ("sx", "sc")
    chan = ("cy", "cz")
    return jax.shard_map(
        shards,
        mesh=grid,
        in_specs=(
            P(chan, seq),
            P(chan, seq),
            P(chan, seq),
            P(None, None, chan),
            P(chan, seq),
            P(chan),
            P(chan, None),
        ),
        out_specs=P(chan, seq),
        check_vma=False,
    )
```

```python
import numpy as np

import jax
import jax.numpy as jnp
from jax.experimental import pallas as pl
from jax.experimental.pallas import tpu as pltpu
from jax import lax
from jax.sharding import Mesh, PartitionSpec as P

INTERPRET = False
BLOCK = 256


def from_behind(value, axis, by):
    count = lax.axis_size(axis)
    pairs = [(i, i + by) for i in range(count) if 0 <= i + by < count]
    return lax.ppermute(value, axis, pairs)


def dft_tables(seq_length):
    rows = 2 * seq_length // BLOCK
    half = seq_length // BLOCK
    k1 = np.arange(rows)[:, None]
    n1 = np.arange(half)[None, :]
    col = np.arange(BLOCK)
    first = 2.0 * np.pi * ((k1 * n1) % rows) / rows
    second = 2.0 * np.pi * ((col[:, None] * col[None, :]) % BLOCK) / BLOCK
    turn = 2.0 * np.pi * (k1 * col[None, :]) / (2 * seq_length)

    def halves(table):
        table = np.asarray(table, np.float32)
        high = table.astype(jnp.bfloat16)
        low = (table - high.astype(np.float32)).astype(jnp.bfloat16)
        return [jnp.asarray(high), jnp.asarray(low)]

    tables = []
    for table in (np.cos(first), np.sin(first), np.cos(second), np.sin(second), np.cos(first).T, np.sin(first).T):
        tables += halves(table)
    tables += [jnp.asarray(np.cos(turn), jnp.float32), jnp.asarray(np.sin(turn), jnp.float32)]
    return tables


def split3(value):
    high = value.astype(jnp.bfloat16)
    return high, (value - high.astype(jnp.float32)).astype(jnp.bfloat16)


def dot3(a, b):
    def one(p, q):
        return jnp.dot(p, q, preferred_element_type=jnp.float32)

    return one(a[0], b[0]) + (one(a[0], b[1]) + one(a[1], b[0]))


def conv_kernel(x_ref, f_ref, c1h, c1l, s1h, s1l, c2h, c2l, s2h, s2l, c1th, c1tl, s1th, s1tl, ct_ref, st_ref, o_ref):
    channels = o_ref.shape[0]
    scale = 1.0 / (2 * x_ref.shape[1] * x_ref.shape[2])
    sources = [x_ref.at[channel] for channel in range(channels)] + [f_ref.at[channel] for channel in range(channels)]
    c1, s1 = (c1h[...], c1l[...]), (s1h[...], s1l[...])
    c2, s2 = (c2h[...], c2l[...]), (s2h[...], s2l[...])
    ct, st = ct_ref[...], st_ref[...]
    spectra = []
    for signal in range(2 * channels):
        piece = split3(sources[signal][...])
        a_re = dot3(c1, piece)
        a_im = -dot3(s1, piece)
        t_re = split3(a_re * ct + a_im * st)
        t_im = split3(a_im * ct - a_re * st)
        spectra.append((dot3(t_re, c2) + dot3(t_im, s2), dot3(t_im, c2) - dot3(t_re, s2)))
    c1t, s1t = (c1th[...], c1tl[...]), (s1th[...], s1tl[...])
    for channel in range(channels):
        (x_re, x_im), (h_re, h_im) = spectra[channel], spectra[channels + channel]
        p_re = split3(x_re * h_re - x_im * h_im)
        p_im = split3(x_re * h_im + x_im * h_re)
        q_re = dot3(p_re, c2) - dot3(p_im, s2)
        q_im = dot3(p_im, c2) + dot3(p_re, s2)
        u_re = split3(q_re * ct - q_im * st)
        u_im = split3(q_im * ct + q_re * st)
        o_ref[channel] = (dot3(c1t, u_re) - dot3(s1t, u_im)) * scale


def spectral_conv(series, filters):
    channels, seq_length = series.shape
    half = seq_length // BLOCK
    rows = 2 * half
    tables = dft_tables(seq_length)
    signal_flops = 3 * 2 * (2 * rows * half * BLOCK + 4 * rows * BLOCK * BLOCK)
    out = pl.pallas_call(
        conv_kernel,
        out_shape=jax.ShapeDtypeStruct((channels, half, BLOCK), jnp.float32),
        compiler_params=pltpu.CompilerParams(vmem_limit_bytes=100 * 1024 * 1024),
        cost_estimate=pl.CostEstimate(
            flops=3 * channels * signal_flops,
            transcendentals=0,
            bytes_accessed=(3 * channels * half * BLOCK + 6 * rows * BLOCK) * 4,
        ),
        interpret=INTERPRET,
    )(series.reshape(channels, half, BLOCK), filters.reshape(channels, half, BLOCK), *tables)
    return out.reshape(channels, seq_length)


def whole_conv(key_value, long_filter):
    joined = jnp.stack([key_value, long_filter])
    regrouped = lax.all_to_all(joined, ("sx", "sc"), split_axis=1, concat_axis=2, tiled=True)
    series = spectral_conv(regrouped[0], regrouped[1])
    return lax.all_to_all(series, ("sx", "sc"), split_axis=1, concat_axis=0, tiled=True)


def shift(value, axis, by):
    count = lax.axis_size(axis)
    return lax.ppermute(value, axis, [(i, (i + by) % count) for i in range(count)])


def ring_gather(piece, axis, split_axis):
    count = lax.axis_size(axis)
    ahead, behind = [piece], [piece]
    for _ in range((count - 1) // 2):
        ahead.append(shift(ahead[-1], axis, -1))
        behind.append(shift(behind[-1], axis, 1))
    order = ahead
    if count % 2 == 0:
        cut = piece.shape[split_axis] // 2
        low = shift(lax.slice_in_dim(behind[-1], 0, cut, axis=split_axis), axis, 1)
        high = shift(lax.slice_in_dim(ahead[-1], cut, None, axis=split_axis), axis, -1)
        order = order + [jnp.concatenate([low, high], axis=split_axis)]
    order = order + behind[1:][::-1]
    return jnp.stack(order)


def rolled_weight(output_weight, first, second):
    rows = output_weight.shape[0]
    size_y, size_z = lax.axis_size("cy"), lax.axis_size("cz")
    grid = output_weight.reshape(rows, size_y, size_z, -1)
    grid = jnp.roll(grid, -lax.axis_index("cy"), axis=1)
    grid = jnp.roll(grid, -lax.axis_index("cz"), axis=2)
    if first == "cy":
        grid = jnp.swapaxes(grid, 1, 2)
    return grid.reshape(rows, -1)


def project(gated, output_weight):
    positions = gated.shape[1]
    cut = positions * 9 // 16
    results = []
    for first, second, part in (("cz", "cy", gated[:, :cut]), ("cy", "cz", gated[:, cut:])):
        inner = ring_gather(part, first, 1)
        outer = ring_gather(inner, second, 2)
        stacked = outer.reshape(-1, part.shape[1])
        weight = rolled_weight(output_weight, first, second)
        results.append(jnp.dot(weight, stacked, preferred_element_type=jnp.float32).astype(jnp.bfloat16))
    return jnp.concatenate(results, axis=1)


def shards(query_input, key_input, value_input, short_taps, long_filter, skip_gain, output_weight):
    channels, positions = query_input.shape
    stacked = jnp.stack([query_input, key_input, value_input])
    before = from_behind(stacked[:, :, positions - 2 :], ("sx", "sc"), 1)
    extended = jnp.concatenate([before, stacked], axis=2).astype(jnp.float32)
    featured = (
        short_taps[0][:, :, None] * extended[:, :, 2:]
        + short_taps[1][:, :, None] * extended[:, :, 1:-1]
        + short_taps[2][:, :, None] * extended[:, :, :-2]
    )
    query_part = featured[0]
    key_value = featured[1] * featured[2]
    convolved = whole_conv(key_value, long_filter)
    gated = (query_part * (convolved + skip_gain[:, None] * key_value)).astype(jnp.bfloat16)
    return project(gated, output_weight)


def solution(mesh):
    seq_size, chan_size = mesh.devices.shape
    z_size = 8 if chan_size % 8 == 0 else chan_size
    grid = Mesh(
        mesh.devices.reshape(seq_size // 2, 2, chan_size // z_size, z_size),
        ("sx", "sc", "cy", "cz"),
    )
    seq = ("sx", "sc")
    chan = ("cy", "cz")
    return jax.shard_map(
        shards,
        mesh=grid,
        in_specs=(
            P(chan, seq),
            P(chan, seq),
            P(chan, seq),
            P(None, None, chan),
            P(chan, seq),
            P(chan),
            P(chan, None),
        ),
        out_specs=P(chan, seq),
        check_vma=False,
    )
```

```python
import numpy as np

import jax
import jax.numpy as jnp
from jax.experimental import pallas as pl
from jax.experimental.pallas import tpu as pltpu
from jax import lax
from jax.sharding import Mesh, PartitionSpec as P

INTERPRET = False
BLOCK = 256


def from_behind(value, axis, by):
    count = lax.axis_size(axis)
    pairs = [(i, i + by) for i in range(count) if 0 <= i + by < count]
    return lax.ppermute(value, axis, pairs)


def dft_tables(seq_length):
    rows = 2 * seq_length // BLOCK
    half = seq_length // BLOCK
    k1 = np.arange(rows)[:, None]
    n1 = np.arange(half)[None, :]
    col = np.arange(BLOCK)
    first = 2.0 * np.pi * ((k1 * n1) % rows) / rows
    second = 2.0 * np.pi * ((col[:, None] * col[None, :]) % BLOCK) / BLOCK
    turn = 2.0 * np.pi * (k1 * col[None, :]) / (2 * seq_length)

    def halves(table):
        table = np.asarray(table, np.float32)
        high = table.astype(jnp.bfloat16)
        low = (table - high.astype(np.float32)).astype(jnp.bfloat16)
        return [jnp.asarray(high), jnp.asarray(low)]

    tables = []
    for table in (np.cos(first), np.sin(first), np.cos(second), np.sin(second), np.cos(first).T, np.sin(first).T):
        tables += halves(table)
    tables += [jnp.asarray(np.cos(turn), jnp.float32), jnp.asarray(np.sin(turn), jnp.float32)]
    return tables


def split3(value):
    high = value.astype(jnp.bfloat16)
    return high, (value - high.astype(jnp.float32)).astype(jnp.bfloat16)


def dot3(a, b):
    def one(p, q):
        return jnp.dot(p, q, preferred_element_type=jnp.float32)

    return one(a[0], b[0]) + (one(a[0], b[1]) + one(a[1], b[0]))


def conv_kernel(x_ref, f_ref, c1h, c1l, s1h, s1l, c2h, c2l, s2h, s2l, c1th, c1tl, s1th, s1tl, ct_ref, st_ref, o_ref):
    channels = o_ref.shape[0]
    scale = 1.0 / (2 * x_ref.shape[1] * x_ref.shape[2])
    sources = [x_ref.at[channel] for channel in range(channels)] + [f_ref.at[channel] for channel in range(channels)]
    c1, s1 = (c1h[...], c1l[...]), (s1h[...], s1l[...])
    c2, s2 = (c2h[...], c2l[...]), (s2h[...], s2l[...])
    ct, st = ct_ref[...], st_ref[...]
    spectra = []
    for signal in range(2 * channels):
        piece = split3(sources[signal][...])
        a_re = dot3(c1, piece)
        a_im = -dot3(s1, piece)
        t_re = split3(a_re * ct + a_im * st)
        t_im = split3(a_im * ct - a_re * st)
        spectra.append((dot3(t_re, c2) + dot3(t_im, s2), dot3(t_im, c2) - dot3(t_re, s2)))
    c1t, s1t = (c1th[...], c1tl[...]), (s1th[...], s1tl[...])
    for channel in range(channels):
        (x_re, x_im), (h_re, h_im) = spectra[channel], spectra[channels + channel]
        p_re = split3(x_re * h_re - x_im * h_im)
        p_im = split3(x_re * h_im + x_im * h_re)
        q_re = dot3(p_re, c2) - dot3(p_im, s2)
        q_im = dot3(p_im, c2) + dot3(p_re, s2)
        u_re = split3(q_re * ct - q_im * st)
        u_im = split3(q_im * ct + q_re * st)
        o_ref[channel] = (dot3(c1t, u_re) - dot3(s1t, u_im)) * scale


def spectral_conv(series, filters):
    channels, seq_length = series.shape
    half = seq_length // BLOCK
    rows = 2 * half
    tables = dft_tables(seq_length)
    signal_flops = 3 * 2 * (2 * rows * half * BLOCK + 4 * rows * BLOCK * BLOCK)
    out = pl.pallas_call(
        conv_kernel,
        out_shape=jax.ShapeDtypeStruct((channels, half, BLOCK), jnp.float32),
        compiler_params=pltpu.CompilerParams(vmem_limit_bytes=100 * 1024 * 1024),
        cost_estimate=pl.CostEstimate(
            flops=3 * channels * signal_flops,
            transcendentals=0,
            bytes_accessed=(3 * channels * half * BLOCK + 6 * rows * BLOCK) * 4,
        ),
        interpret=INTERPRET,
    )(series.reshape(channels, half, BLOCK), filters.reshape(channels, half, BLOCK), *tables)
    return out.reshape(channels, seq_length)


def whole_conv(key_value, long_filter):
    joined = jnp.stack([key_value, long_filter])
    regrouped = lax.all_to_all(joined, ("sx", "sc"), split_axis=1, concat_axis=2, tiled=True)
    series = spectral_conv(regrouped[0], regrouped[1])
    return lax.all_to_all(series, ("sx", "sc"), split_axis=1, concat_axis=0, tiled=True)


def shift(value, axis, by):
    count = lax.axis_size(axis)
    return lax.ppermute(value, axis, [(i, (i + by) % count) for i in range(count)])


def ring_gather(piece, axis, split_axis):
    count = lax.axis_size(axis)
    ahead, behind = [piece], [piece]
    for _ in range((count - 1) // 2):
        ahead.append(shift(ahead[-1], axis, -1))
        behind.append(shift(behind[-1], axis, 1))
    order = ahead
    if count % 2 == 0:
        cut = piece.shape[split_axis] // 2
        low = shift(lax.slice_in_dim(behind[-1], 0, cut, axis=split_axis), axis, 1)
        high = shift(lax.slice_in_dim(ahead[-1], cut, None, axis=split_axis), axis, -1)
        order = order + [jnp.concatenate([low, high], axis=split_axis)]
    order = order + behind[1:][::-1]
    return jnp.stack(order)


def rolled_weight(output_weight, first, second):
    rows = output_weight.shape[0]
    size_y, size_z = lax.axis_size("cy"), lax.axis_size("cz")
    grid = output_weight.reshape(rows, size_y, size_z, -1)
    grid = jnp.roll(grid, -lax.axis_index("cy"), axis=1)
    grid = jnp.roll(grid, -lax.axis_index("cz"), axis=2)
    if first == "cy":
        grid = jnp.swapaxes(grid, 1, 2)
    return grid.reshape(rows, -1)


def project(gated, output_weight):
    positions = gated.shape[1]
    cut = positions * 19 // 32
    results = []
    for first, second, part in (("cz", "cy", gated[:, :cut]), ("cy", "cz", gated[:, cut:])):
        inner = ring_gather(part, first, 1)
        outer = ring_gather(inner, second, 2)
        stacked = outer.reshape(-1, part.shape[1])
        weight = rolled_weight(output_weight, first, second)
        results.append(jnp.dot(weight, stacked, preferred_element_type=jnp.float32).astype(jnp.bfloat16))
    return jnp.concatenate(results, axis=1)


def shards(query_input, key_input, value_input, short_taps, long_filter, skip_gain, output_weight):
    channels, positions = query_input.shape
    stacked = jnp.stack([query_input, key_input, value_input])
    before = from_behind(stacked[:, :, positions - 2 :], ("sx", "sc"), 1)
    extended = jnp.concatenate([before, stacked], axis=2).astype(jnp.float32)
    featured = (
        short_taps[0][:, :, None] * extended[:, :, 2:]
        + short_taps[1][:, :, None] * extended[:, :, 1:-1]
        + short_taps[2][:, :, None] * extended[:, :, :-2]
    )
    query_part = featured[0]
    key_value = featured[1] * featured[2]
    convolved = whole_conv(key_value, long_filter)
    gated = (query_part * (convolved + skip_gain[:, None] * key_value)).astype(jnp.bfloat16)
    return project(gated, output_weight)


def solution(mesh):
    seq_size, chan_size = mesh.devices.shape
    z_size = 8 if chan_size % 8 == 0 else chan_size
    grid = Mesh(
        mesh.devices.reshape(seq_size // 2, 2, chan_size // z_size, z_size),
        ("sx", "sc", "cy", "cz"),
    )
    seq = ("sx", "sc")
    chan = ("cy", "cz")
    return jax.shard_map(
        shards,
        mesh=grid,
        in_specs=(
            P(chan, seq),
            P(chan, seq),
            P(chan, seq),
            P(None, None, chan),
            P(chan, seq),
            P(chan),
            P(chan, None),
        ),
        out_specs=P(chan, seq),
        check_vma=False,
    )
```

```python
import numpy as np

import jax
import jax.numpy as jnp
from jax.experimental import pallas as pl
from jax.experimental.pallas import tpu as pltpu
from jax import lax
from jax.sharding import Mesh, PartitionSpec as P

INTERPRET = False
BLOCK = 256


def from_behind(value, axis, by):
    count = lax.axis_size(axis)
    pairs = [(i, i + by) for i in range(count) if 0 <= i + by < count]
    return lax.ppermute(value, axis, pairs)


def dft_tables(seq_length):
    rows = 2 * seq_length // BLOCK
    half = seq_length // BLOCK
    k1 = np.arange(rows)[:, None]
    n1 = np.arange(half)[None, :]
    col = np.arange(BLOCK)
    first = 2.0 * np.pi * ((k1 * n1) % rows) / rows
    second = 2.0 * np.pi * ((col[:, None] * col[None, :]) % BLOCK) / BLOCK
    turn = 2.0 * np.pi * (k1 * col[None, :]) / (2 * seq_length)

    def halves(table):
        table = np.asarray(table, np.float32)
        high = table.astype(jnp.bfloat16)
        low = (table - high.astype(np.float32)).astype(jnp.bfloat16)
        return [jnp.asarray(high), jnp.asarray(low)]

    tables = []
    for table in (np.cos(first), np.sin(first), np.cos(second), np.sin(second), np.cos(first).T, np.sin(first).T):
        tables += halves(table)
    tables += [jnp.asarray(np.cos(turn), jnp.float32), jnp.asarray(np.sin(turn), jnp.float32)]
    return tables


def split3(value):
    high = value.astype(jnp.bfloat16)
    return high, (value - high.astype(jnp.float32)).astype(jnp.bfloat16)


def dot3(a, b):
    def one(p, q):
        return jnp.dot(p, q, preferred_element_type=jnp.float32)

    return one(a[0], b[0]) + (one(a[0], b[1]) + one(a[1], b[0]))


def conv_kernel(x_ref, c1h, c1l, s1h, s1l, c2h, c2l, s2h, s2l, c1th, c1tl, s1th, s1tl, ct_ref, st_ref, o_ref):
    channels = o_ref.shape[0]
    scale = 1.0 / (2 * x_ref.shape[1] * x_ref.shape[2])
    c1, s1 = (c1h[...], c1l[...]), (s1h[...], s1l[...])
    c2, s2 = (c2h[...], c2l[...]), (s2h[...], s2l[...])
    ct, st = ct_ref[...], st_ref[...]
    spectra = []
    for signal in range(2 * channels):
        piece = split3(x_ref[signal])
        a_re = dot3(c1, piece)
        a_im = -dot3(s1, piece)
        t_re = split3(a_re * ct + a_im * st)
        t_im = split3(a_im * ct - a_re * st)
        spectra.append((dot3(t_re, c2) + dot3(t_im, s2), dot3(t_im, c2) - dot3(t_re, s2)))
    c1t, s1t = (c1th[...], c1tl[...]), (s1th[...], s1tl[...])
    for channel in range(channels):
        (x_re, x_im), (h_re, h_im) = spectra[channel], spectra[channels + channel]
        p_re = split3(x_re * h_re - x_im * h_im)
        p_im = split3(x_re * h_im + x_im * h_re)
        q_re = dot3(p_re, c2) - dot3(p_im, s2)
        q_im = dot3(p_im, c2) + dot3(p_re, s2)
        u_re = split3(q_re * ct - q_im * st)
        u_im = split3(q_im * ct + q_re * st)
        o_ref[channel] = (dot3(c1t, u_re) - dot3(s1t, u_im)) * scale


def spectral_conv(series, filters):
    channels, seq_length = series.shape
    half = seq_length // BLOCK
    rows = 2 * half
    stacked = jnp.concatenate([series, filters]).reshape(2 * channels, half, BLOCK)
    tables = dft_tables(seq_length)
    signal_flops = 3 * 2 * (2 * rows * half * BLOCK + 4 * rows * BLOCK * BLOCK)
    out = pl.pallas_call(
        conv_kernel,
        out_shape=jax.ShapeDtypeStruct((channels, half, BLOCK), jnp.float32),
        compiler_params=pltpu.CompilerParams(vmem_limit_bytes=100 * 1024 * 1024),
        cost_estimate=pl.CostEstimate(
            flops=3 * channels * signal_flops,
            transcendentals=0,
            bytes_accessed=(3 * channels * half * BLOCK + 6 * rows * BLOCK) * 4,
        ),
        interpret=INTERPRET,
    )(stacked, *tables)
    return out.reshape(channels, seq_length)


def whole_conv(key_value, long_filter):
    joined = jnp.stack([key_value, long_filter])
    regrouped = lax.all_to_all(joined, ("sx", "sc"), split_axis=1, concat_axis=2, tiled=True)
    series = spectral_conv(regrouped[0], regrouped[1])
    sent = lax.all_to_all(series.astype(jnp.bfloat16), ("sx", "sc"), split_axis=1, concat_axis=0, tiled=True)
    return sent.astype(jnp.float32)


def shift(value, axis, by):
    count = lax.axis_size(axis)
    return lax.ppermute(value, axis, [(i, (i + by) % count) for i in range(count)])


def ring_gather(piece, axis, split_axis):
    count = lax.axis_size(axis)
    ahead, behind = [piece], [piece]
    for _ in range((count - 1) // 2):
        ahead.append(shift(ahead[-1], axis, -1))
        behind.append(shift(behind[-1], axis, 1))
    order = ahead
    if count % 2 == 0:
        cut = piece.shape[split_axis] // 2
        low = shift(lax.slice_in_dim(behind[-1], 0, cut, axis=split_axis), axis, 1)
        high = shift(lax.slice_in_dim(ahead[-1], cut, None, axis=split_axis), axis, -1)
        order = order + [jnp.concatenate([low, high], axis=split_axis)]
    order = order + behind[1:][::-1]
    return jnp.stack(order)


def rolled_weight(output_weight, first, second):
    rows = output_weight.shape[0]
    size_y, size_z = lax.axis_size("cy"), lax.axis_size("cz")
    grid = output_weight.reshape(rows, size_y, size_z, -1)
    grid = jnp.roll(grid, -lax.axis_index("cy"), axis=1)
    grid = jnp.roll(grid, -lax.axis_index("cz"), axis=2)
    if first == "cy":
        grid = jnp.swapaxes(grid, 1, 2)
    return grid.reshape(rows, -1)


def project(gated, output_weight):
    positions = gated.shape[1]
    cut = positions * 9 // 16
    results = []
    for first, second, part in (("cz", "cy", gated[:, :cut]), ("cy", "cz", gated[:, cut:])):
        inner = ring_gather(part, first, 1)
        outer = ring_gather(inner, second, 2)
        stacked = outer.reshape(-1, part.shape[1])
        weight = rolled_weight(output_weight, first, second)
        results.append(jnp.dot(weight, stacked, preferred_element_type=jnp.float32))
    return jnp.concatenate(results, axis=1).astype(jnp.bfloat16)


def shards(query_input, key_input, value_input, short_taps, long_filter, skip_gain, output_weight):
    channels, positions = query_input.shape
    stacked = jnp.stack([query_input, key_input, value_input])
    before = from_behind(stacked[:, :, positions - 2 :], ("sx", "sc"), 1)
    extended = jnp.concatenate([before, stacked], axis=2).astype(jnp.float32)
    featured = (
        short_taps[0][:, :, None] * extended[:, :, 2:]
        + short_taps[1][:, :, None] * extended[:, :, 1:-1]
        + short_taps[2][:, :, None] * extended[:, :, :-2]
    )
    query_part = featured[0]
    key_value = featured[1] * featured[2]
    convolved = whole_conv(key_value, long_filter)
    gated = (query_part * (convolved + skip_gain[:, None] * key_value)).astype(jnp.bfloat16)
    return project(gated, output_weight)


def solution(mesh):
    seq_size, chan_size = mesh.devices.shape
    z_size = 8 if chan_size % 8 == 0 else chan_size
    grid = Mesh(
        mesh.devices.reshape(seq_size // 2, 2, chan_size // z_size, z_size),
        ("sx", "sc", "cy", "cz"),
    )
    seq = ("sx", "sc")
    chan = ("cy", "cz")
    return jax.shard_map(
        shards,
        mesh=grid,
        in_specs=(
            P(chan, seq),
            P(chan, seq),
            P(chan, seq),
            P(None, None, chan),
            P(chan, seq),
            P(chan),
            P(chan, None),
        ),
        out_specs=P(chan, seq),
        check_vma=False,
    )
```
